128 devices in a mesh: blk: 16 (over x_lo, y, core), col: 8 (over x_hi, z).
Axes of the slice: x: 4 (x_hi: 2, x_lo: 2; x = x_hi * 2 + x_lo), y: 4, z: 4, core: 2. Of those that a mesh axis runs over, the one named last changes fastest.
Arguments:
- queries: bfloat16 [2048, 384], P('blk', 'col'), may hold values from -8 to 8
- key_proj: bfloat16 [2048, 384], P('blk', 'col'), may hold values from -8 to 8
- value_proj: bfloat16 [2048, 384], P('blk', 'col'), may hold values from -6 to 6
- out_grad: bfloat16 [2048, 384], P('blk', 'col'), may hold values from -12 to 12
- pair_rep: bfloat16 [2048, 2048, 128], P('blk', 'col'), may hold values from -600 to 600
- norm_gain: float32 [128], replicated, may hold values from 0.1 to 1.9
- bias_weight: bfloat16 [128, 16], replicated, may hold values from -1 to 1
- chain_ids: int32 [2048], replicated, may hold values from 0 to 15, never falling along the last dimension, each value on 1 to 512 neighbouring positions
- block_mask: int32 [16, 16], replicated, may hold values 0 or 1
Outputs:
- grad_queries: bfloat16 [2048, 384], P('blk', 'col')
- grad_keys: bfloat16 [2048, 384], P('blk', 'col')
- grad_values: bfloat16 [2048, 384], P('blk', 'col')
- grad_pair: bfloat16 [2048, 2048, 128], P('blk', 'col')
- grad_gain: float32 [128], replicated
- grad_weight: float32 [128, 16], replicated
The draws below stay inside these ranges and needn't reach their ends.
Inputs may be any that keep to these rules, and one draw needn't show every extreme that they name: `chain_ids`: chain ids never fall along the tokens; every chain has 1 to 512 tokens and one has exactly 512.
All inputs are finite; a program needn't handle non-finite values.
Results may differ from the reference program's by a relative error of at most 0.02.
Values may be sent and summed in bfloat16 or wider, within the bound.
No kernel may reach another device: no remote copies, remote signals or barrier semaphores. Data moves between devices by JAX's collectives and lax.ppermute only.
A program may use at most 192 MiB of HBM per device.

```python
import math
import jax
import jax.numpy as jnp
import numpy as np
from jax import lax

HEADS = 16
HEAD_DIM = 24
PAIR = 128
WIDTH = 384
TOK_DEV = 128
TOKENS = 2048
MASK_BLOCK = 128
MBLOCKS = 16
CHAINS = 16
CHAIN_MOST = 512


def drawn_pair(key):
    first = jax.random.fold_in(key, 7101)
    second = jax.random.fold_in(key, 7102)
    shape = (TOKENS, HEADS * HEAD_DIM)
    query_draw = jnp.clip(jax.random.normal(first, shape, jnp.float32), -4.0, 4.0)
    key_draw = jnp.clip(jax.random.normal(second, shape, jnp.float32), -4.0, 4.0)
    return (query_draw, key_draw)


def draw_queries(key, part):
    return drawn_pair(key)[0].astype(jnp.bfloat16)


def draw_key_proj(key, part):
    return drawn_pair(key)[1].astype(jnp.bfloat16)


def draw_pair_rep(key, part):
    first = jax.random.fold_in(key, 8201)
    second = jax.random.fold_in(key, 8202)
    third = jax.random.fold_in(key, 8203)
    shape = (TOKENS, TOKENS, PAIR)
    channel_scale = jnp.exp(jax.random.uniform(third, (PAIR,), jnp.float32, 0.0, math.log(10.0)))
    base = jnp.clip(jax.random.normal(first, shape, jnp.float32), -4.0, 4.0)
    row_scale = jnp.exp(jax.random.uniform(second, (TOKENS, TOKENS, 1), jnp.float32, 0.0, math.log(10.0)))
    return (base * row_scale * channel_scale).astype(jnp.bfloat16)


def with_ends(drawn, own_key, least, high):
    index_at = [jax.random.randint(jax.random.fold_in(own_key, axis), (), 0, length) for axis, length in enumerate(drawn.shape)]
    longest = drawn.shape.index(max(drawn.shape))
    neighbour = index_at[:longest] + [(index_at[longest] + 1) % drawn.shape[longest]] + index_at[longest + 1:]
    return drawn.at[tuple(index_at)].set(least).at[tuple(neighbour)].set(high)


def block_scale(own_key, extent, pieces, least, largest):
    factor_of, own = 1.0, jax.random.fold_in(own_key, 6)
    for axis_at, blocks in pieces:
        steps = jnp.exp(jax.random.uniform(jax.random.fold_in(own, axis_at), (blocks,), jnp.float32, least / len(pieces), largest / len(pieces)))
        factor_of = factor_of * jnp.repeat(steps, extent[axis_at] // blocks).reshape([-1 if axis == axis_at else 1 for axis in range(len(extent))])
    return factor_of


def profile(count, total, bound, skew):
    loads = [(1 << 20) // math.isqrt(rank ** skew) + 1 for rank in range(2, count + 1)]
    rest, holding = total - bound - (count - 1), [1] * (count - 1)
    while rest > 0:
        free = [i for i in range(count - 1) if holding[i] < bound]
        whole, budget = sum([loads[i] for i in free]), rest
        for i in free:
            more = min(bound - holding[i], max(1, budget * loads[i] // whole), rest)
            holding[i] = holding[i] + more
            rest = rest - more
    return np.array([bound] + holding)


def ragged(rng, number_of, total, most, lean):
    if number_of == 2:
        one = jax.random.randint(rng, (), max(1, total - most), min(most, total - 1) + 1)
        return jnp.stack([one, total - one])
    tallies = jnp.asarray(profile(number_of, total, most, lean), jnp.int32)
    couples = (number_of - 1) // 2
    giver, taker = tallies[1:1 + 2 * couples:2], tallies[2:2 + 2 * couples:2]
    room = jnp.minimum(giver - 1, most - taker)
    moved = jax.random.randint(jax.random.fold_in(rng, 1), (couples,), 0, 1 << 20) % (room + 1)
    tallies = tallies.at[1:1 + 2 * couples:2].set(giver - moved).at[2:2 + 2 * couples:2].set(taker + moved)
    return tallies[jax.random.permutation(jax.random.fold_in(rng, 2), number_of)]


def normal_values(own_key, shape, spread, bound, cuts=(), kind=jnp.bfloat16):
    entries = spread * jax.random.normal(own_key, shape, jnp.float32)
    if cuts:
        entries = entries * block_scale(own_key, shape, cuts, -0.22, 0.18)
    return jnp.clip(entries, -bound, bound).astype(kind)


def setup_inputs(seed: int = 0) -> dict:
    key_list = jax.random.split(jax.random.key(seed), 10)
    queries = draw_queries(jax.random.fold_in(key_list[9], 71), 0)
    key_proj = draw_key_proj(jax.random.fold_in(key_list[9], 71), 0)
    value_proj = normal_values(key_list[2], (TOKENS, WIDTH), 1.0, 6.0, ((0, 16), (1, 8)))
    out_grad = normal_values(key_list[3], (TOKENS, WIDTH), 2.0, 12.0, ((0, 16), (1, 8)))
    pair_rep = draw_pair_rep(jax.random.fold_in(key_list[9], 71), 0)
    norm_gain = jnp.clip(1.0 + 0.18 * jax.random.normal(key_list[5], (PAIR,), jnp.float32), 0.1, 1.9)
    bias_weight = normal_values(key_list[6], (PAIR, HEADS), 32 ** -0.5, 1.0)
    chain_ids = jnp.searchsorted(jnp.cumsum(ragged(key_list[7], CHAINS, TOKENS, CHAIN_MOST, 2)), jnp.arange(TOKENS), side="right").astype(jnp.int32)
    block_mask = with_ends((jax.random.randint(key_list[8], (MBLOCKS, MBLOCKS), 0, 2) < 1).astype(jnp.int32), jax.random.fold_in(key_list[8], 1), 0, 1)
    return {"queries": queries, "key_proj": key_proj, "value_proj": value_proj, "out_grad": out_grad, "pair_rep": pair_rep, "norm_gain": norm_gain, "bias_weight": bias_weight, "chain_ids": chain_ids, "block_mask": block_mask}


def pair_norm(pair_rows, norm_gain):
    values = pair_rows.astype(jnp.float32)
    centre = lax.optimization_barrier(jnp.mean(values, axis=-1, keepdims=True))
    shifted = values - centre
    inverse = lax.rsqrt(lax.optimization_barrier(jnp.mean(shifted * shifted, axis=-1, keepdims=True)) + 1e-05)
    unit = shifted * inverse
    normed = (unit * norm_gain.astype(jnp.float32)).astype(jnp.bfloat16)
    return (unit, inverse, normed)

def rounded(values):
    return lax.optimization_barrier(values.astype(jnp.bfloat16)).astype(jnp.float32)

def reference(queries, key_proj, value_proj, out_grad, pair_rep, norm_gain, bias_weight, chain_ids, block_mask):
    scale_factor = 1.0 / math.sqrt(HEAD_DIM)
    query_heads = queries.astype(jnp.float32).reshape(TOKENS, HEADS, HEAD_DIM)
    key_heads = key_proj.astype(jnp.float32).reshape(TOKENS, HEADS, HEAD_DIM)
    value_heads = value_proj.astype(jnp.float32).reshape(TOKENS, HEADS, HEAD_DIM)
    grad_heads = out_grad.astype(jnp.float32).reshape(TOKENS, HEADS, HEAD_DIM)
    weight_float = bias_weight.astype(jnp.float32)
    gain_float = norm_gain.astype(jnp.float32)
    columns = jnp.arange(TOKENS, dtype=jnp.int32)
    column_blocks = columns // MASK_BLOCK

    def one_block(carry, block_index):
        key_acc, value_acc, weight_acc, gain_acc = carry
        start = (block_index * TOK_DEV).astype(jnp.int32)
        pair_rows = lax.dynamic_slice_in_dim(pair_rep, start, TOK_DEV, 0)
        unit, inverse, normed = pair_norm(pair_rows, norm_gain)
        normed_float = lax.optimization_barrier(normed).astype(jnp.float32)
        bias = rounded(jnp.einsum('ijc,ch->hij', normed_float, weight_float))
        rows = start + jnp.arange(TOK_DEV, dtype=jnp.int32)
        block_rows = jnp.take(block_mask, rows // MASK_BLOCK, axis=0)
        hits = jnp.take(block_rows, column_blocks, axis=1) > 0
        chain_rows = jnp.take(chain_ids, rows)
        allowed = hits | (chain_rows[:, None] == chain_ids[None, :])
        query_block = lax.dynamic_slice_in_dim(query_heads, start, TOK_DEV, 0)
        grad_block = lax.dynamic_slice_in_dim(grad_heads, start, TOK_DEV, 0)
        scores = jnp.einsum('qhd,khd->hqk', query_block, key_heads) * scale_factor + bias
        masked = jnp.where(allowed[None], scores, -jnp.inf)
        row_top = lax.optimization_barrier(jnp.max(masked, axis=-1, keepdims=True))
        expo = jnp.where(allowed[None], jnp.exp(masked - row_top), 0.0)
        log_total = row_top + jnp.log(lax.optimization_barrier(jnp.sum(expo, axis=-1, keepdims=True)))
        weights = jnp.where(allowed[None], jnp.exp(masked - log_total), 0.0)
        probs = rounded(weights)
        attended = jnp.einsum('hqk,khd->qhd', weights, value_heads)
        delta = lax.optimization_barrier(jnp.sum(grad_block * attended, axis=-1)).T
        dprobs = jnp.einsum('qhd,khd->hqk', grad_block, value_heads)
        dscores = rounded(probs * (dprobs - delta[:, :, None]))
        grad_query_block = (jnp.einsum('hqk,khd->qhd', dscores, key_heads) * scale_factor).reshape(TOK_DEV, WIDTH).astype(jnp.bfloat16)
        key_acc = key_acc + jnp.einsum('hqk,qhd->khd', dscores, query_block) * scale_factor
        value_acc = value_acc + jnp.einsum('hqk,qhd->khd', probs, grad_block)
        dnormed = jnp.einsum('hij,ch->ijc', dscores, weight_float)
        gain_acc = gain_acc + lax.optimization_barrier(jnp.sum(dnormed * unit, axis=(0, 1)))
        weight_acc = weight_acc + jnp.einsum('ijc,hij->ch', normed_float, dscores)
        scaled = dnormed * gain_float
        grad_pair_block = inverse * (scaled - lax.optimization_barrier(jnp.mean(scaled, axis=-1, keepdims=True)) - unit * lax.optimization_barrier(jnp.mean(scaled * unit, axis=-1, keepdims=True)))
        return ((key_acc, value_acc, weight_acc, gain_acc), (grad_query_block, grad_pair_block.astype(jnp.bfloat16)))
    initial = (jnp.zeros((TOKENS, HEADS, HEAD_DIM), jnp.float32), jnp.zeros((TOKENS, HEADS, HEAD_DIM), jnp.float32), jnp.zeros((PAIR, HEADS), jnp.float32), jnp.zeros((PAIR,), jnp.float32))
    finals, stacked = lax.scan(one_block, initial, jnp.arange(TOKENS // TOK_DEV, dtype=jnp.int32))
    key_acc, value_acc, grad_weight, grad_gain = finals
    grad_queries = stacked[0].reshape(TOKENS, WIDTH)
    grad_pair = stacked[1].reshape(TOKENS, TOKENS, PAIR)
    grad_keys = key_acc.reshape(TOKENS, WIDTH).astype(jnp.bfloat16)
    grad_values = value_acc.reshape(TOKENS, WIDTH).astype(jnp.bfloat16)
    return (grad_queries, grad_keys, grad_values, grad_pair, grad_gain, grad_weight)
```

```python
import math

import jax
import jax.numpy as jnp
from jax import lax
from jax.sharding import PartitionSpec as P

HEAD_DIM = 24
MASK_BLOCK = 128


def pair_norm(pair_rows, norm_gain):
    values = pair_rows.astype(jnp.float32)
    centre = jnp.mean(values, axis=-1, keepdims=True)
    shifted = values - centre
    inverse = lax.rsqrt(jnp.mean(shifted * shifted, axis=-1, keepdims=True) + 1e-05)
    unit = shifted * inverse
    normed = (unit * norm_gain).astype(jnp.bfloat16)
    return (unit, inverse, normed)


def block_onehot(first_token, count, nblocks):
    block_ids = (first_token + jnp.arange(count, dtype=jnp.int32)) // MASK_BLOCK
    return (block_ids[:, None] == jnp.arange(nblocks, dtype=jnp.int32)[None, :]).astype(
        jnp.bfloat16
    )


def local(
    queries, key_proj, value_proj, out_grad, pair_rep, norm_gain, bias_weight, chain_ids, block_mask
):
    tok_rows = queries.shape[0]
    local_width = queries.shape[1]
    local_heads = local_width // HEAD_DIM
    scale_factor = 1.0 / math.sqrt(HEAD_DIM)
    blk_index = lax.axis_index("blk")
    blk_count = lax.axis_size("blk")
    all_tokens = blk_count * tok_rows
    row_start = blk_index * tok_rows
    nblocks = block_mask.shape[0]
    rows_table = jnp.dot(
        block_onehot(row_start, tok_rows, nblocks),
        block_mask.astype(jnp.bfloat16),
        preferred_element_type=jnp.float32,
    ).astype(jnp.bfloat16)
    chain_rows = lax.dynamic_slice_in_dim(chain_ids, row_start, tok_rows)
    hits = lax.dot_general(
        rows_table,
        block_onehot(0, all_tokens, nblocks),
        (((1,), (1,)), ((), ())),
        preferred_element_type=jnp.float32,
    )
    allowed = (hits > 0.5) | (chain_rows[:, None] == chain_ids[None, :])

    unit, inverse, normed = pair_norm(pair_rep, norm_gain)
    kv_local = jnp.stack([key_proj, value_proj])
    kv_all = lax.all_gather(kv_local, "blk", axis=1, tiled=True)
    query_heads = queries.reshape(tok_rows, local_heads, HEAD_DIM)
    grad_heads = out_grad.reshape(tok_rows, local_heads, HEAD_DIM)
    key_heads = kv_all[0].reshape(all_tokens, local_heads, HEAD_DIM)
    value_heads = kv_all[1].reshape(all_tokens, local_heads, HEAD_DIM)
    bias_local = jnp.einsum(
        "ijc,ch->hij", normed, bias_weight, preferred_element_type=jnp.float32
    ).astype(jnp.bfloat16)
    bias_mine = lax.all_to_all(bias_local, "col", split_axis=0, concat_axis=2, tiled=True)

    scores = (
        jnp.einsum("qhd,khd->hqk", query_heads, key_heads, preferred_element_type=jnp.float32)
        * scale_factor
        + bias_mine.astype(jnp.float32)
    )
    masked = jnp.where(allowed[None], scores, -jnp.inf)
    row_top = jnp.max(masked, axis=-1, keepdims=True)
    expo = jnp.where(allowed[None], jnp.exp(scores - row_top), 0.0)
    totals = jnp.sum(expo, axis=-1, keepdims=True)
    log_total = row_top + jnp.log(totals)
    weights = jnp.where(allowed[None], jnp.exp(scores - log_total), 0.0)
    probs = weights.astype(jnp.bfloat16)
    attended = jnp.einsum("hqk,khd->qhd", weights, value_heads.astype(jnp.float32))
    delta = jnp.sum(grad_heads.astype(jnp.float32) * attended, axis=-1).T
    dprobs = jnp.einsum(
        "qhd,khd->hqk", grad_heads, value_heads, preferred_element_type=jnp.float32
    )
    dscores = (probs.astype(jnp.float32) * (dprobs - delta[:, :, None])).astype(jnp.bfloat16)
    query_add = (
        jnp.einsum("hqk,khd->qhd", dscores, key_heads, preferred_element_type=jnp.float32)
        * scale_factor
    )
    key_add = (
        jnp.einsum("hqk,qhd->khd", dscores, query_heads, preferred_element_type=jnp.float32)
        * scale_factor
    )
    value_add = jnp.einsum("hqk,qhd->khd", probs, grad_heads, preferred_element_type=jnp.float32)
    kv_part = jnp.stack(
        [key_add.reshape(all_tokens, local_width), value_add.reshape(all_tokens, local_width)]
    )
    kv_grads = lax.psum_scatter(kv_part, "blk", scatter_dimension=1, tiled=True)
    grad_queries = query_add.reshape(tok_rows, local_width).astype(jnp.bfloat16)
    grad_keys = kv_grads[0].astype(jnp.bfloat16)
    grad_values = kv_grads[1].astype(jnp.bfloat16)
    dbias_cells = lax.all_to_all(dscores, "col", split_axis=2, concat_axis=0, tiled=True)
    dnormed = jnp.einsum(
        "hij,ch->ijc", dbias_cells, bias_weight, preferred_element_type=jnp.float32
    )
    gain_part = jnp.sum(dnormed * unit, axis=(0, 1))
    weight_part = jnp.einsum("ijc,hij->ch", normed, dbias_cells, preferred_element_type=jnp.float32)
    pair_width = gain_part.shape[0]
    packed = jnp.concatenate([gain_part, weight_part.reshape(-1)])
    packed = lax.psum(packed, ("blk", "col"))
    grad_gain = packed[:pair_width]
    grad_weight = packed[pair_width:].reshape(weight_part.shape)
    scaled = dnormed * norm_gain
    grad_pair = (
        inverse
        * (
            scaled
            - jnp.mean(scaled, axis=-1, keepdims=True)
            - unit * jnp.mean(scaled * unit, axis=-1, keepdims=True)
        )
    ).astype(jnp.bfloat16)
    return (grad_queries, grad_keys, grad_values, grad_pair, grad_gain, grad_weight)


def solution(mesh):
    placed = (
        P("blk", "col"),
        P("blk", "col"),
        P("blk", "col"),
        P("blk", "col"),
        P("blk", "col", None),
        P(),
        P(),
        P(),
        P(),
    )
    return jax.shard_map(
        local,
        mesh=mesh,
        in_specs=placed,
        out_specs=(
            P("blk", "col"),
            P("blk", "col"),
            P("blk", "col"),
            P("blk", "col", None),
            P(),
            P(),
        ),
        check_vma=False,
    )
```

```python
import math

import jax
import jax.numpy as jnp
from jax import lax
from jax.sharding import PartitionSpec as P

HEAD_DIM = 24
MASK_BLOCK = 128


def pair_norm(pair_rows, norm_gain):
    values = pair_rows.astype(jnp.float32)
    centre = jnp.mean(values, axis=-1, keepdims=True)
    shifted = values - centre
    inverse = lax.rsqrt(jnp.mean(shifted * shifted, axis=-1, keepdims=True) + 1e-05)
    unit = shifted * inverse
    normed = (unit * norm_gain).astype(jnp.bfloat16)
    return (unit, inverse, normed)


def block_onehot(first_token, count, nblocks):
    block_ids = (first_token + jnp.arange(count, dtype=jnp.int32)) // MASK_BLOCK
    return (block_ids[:, None] == jnp.arange(nblocks, dtype=jnp.int32)[None, :]).astype(
        jnp.bfloat16
    )


def local(
    queries, key_proj, value_proj, out_grad, pair_rep, norm_gain, bias_weight, chain_ids, block_mask
):
    tok_rows = queries.shape[0]
    local_width = queries.shape[1]
    local_heads = local_width // HEAD_DIM
    scale_factor = 1.0 / math.sqrt(HEAD_DIM)
    blk_index = lax.axis_index("blk")
    blk_count = lax.axis_size("blk")
    all_tokens = blk_count * tok_rows
    row_start = blk_index * tok_rows
    nblocks = block_mask.shape[0]
    rows_table = jnp.dot(
        block_onehot(row_start, tok_rows, nblocks),
        block_mask.astype(jnp.bfloat16),
        preferred_element_type=jnp.float32,
    ).astype(jnp.bfloat16)
    chain_rows = lax.dynamic_slice_in_dim(chain_ids, row_start, tok_rows)
    hits = lax.dot_general(
        rows_table,
        block_onehot(0, all_tokens, nblocks),
        (((1,), (1,)), ((), ())),
        preferred_element_type=jnp.float32,
    )
    allowed = (hits > 0.5) | (chain_rows[:, None] == chain_ids[None, :])

    unit, inverse, normed = pair_norm(pair_rep, norm_gain)
    kv_local = jnp.stack([key_proj, value_proj])
    kv_rep = jnp.broadcast_to(kv_local[None], (blk_count,) + kv_local.shape)
    kv_all = lax.all_to_all(kv_rep, "blk", split_axis=0, concat_axis=0, tiled=True)
    kv_all = jnp.transpose(kv_all, (1, 0, 2, 3)).reshape(2, all_tokens, local_width)
    query_heads = queries.reshape(tok_rows, local_heads, HEAD_DIM)
    grad_heads = out_grad.reshape(tok_rows, local_heads, HEAD_DIM)
    key_heads = kv_all[0].reshape(all_tokens, local_heads, HEAD_DIM)
    value_heads = kv_all[1].reshape(all_tokens, local_heads, HEAD_DIM)
    bias_local = jnp.einsum(
        "ijc,ch->hij", normed, bias_weight, preferred_element_type=jnp.float32
    ).astype(jnp.bfloat16)
    bias_mine = lax.all_to_all(bias_local, "col", split_axis=0, concat_axis=2, tiled=True)

    scores = (
        jnp.einsum("qhd,khd->hqk", query_heads, key_heads, preferred_element_type=jnp.float32)
        * scale_factor
        + bias_mine.astype(jnp.float32)
    )
    masked = jnp.where(allowed[None], scores, -jnp.inf)
    row_top = jnp.max(masked, axis=-1, keepdims=True)
    expo = jnp.where(allowed[None], jnp.exp(scores - row_top), 0.0)
    totals = jnp.sum(expo, axis=-1, keepdims=True)
    log_total = row_top + jnp.log(totals)
    weights = jnp.where(allowed[None], jnp.exp(scores - log_total), 0.0)
    probs = weights.astype(jnp.bfloat16)
    attended = jnp.einsum("hqk,khd->qhd", weights, value_heads.astype(jnp.float32))
    delta = jnp.sum(grad_heads.astype(jnp.float32) * attended, axis=-1).T
    dprobs = jnp.einsum(
        "qhd,khd->hqk", grad_heads, value_heads, preferred_element_type=jnp.float32
    )
    dscores = (probs.astype(jnp.float32) * (dprobs - delta[:, :, None])).astype(jnp.bfloat16)
    query_add = (
        jnp.einsum("hqk,khd->qhd", dscores, key_heads, preferred_element_type=jnp.float32)
        * scale_factor
    )
    key_add = (
        jnp.einsum("hqk,qhd->khd", dscores, query_heads, preferred_element_type=jnp.float32)
        * scale_factor
    )
    value_add = jnp.einsum("hqk,qhd->khd", probs, grad_heads, preferred_element_type=jnp.float32)
    kv_part = jnp.stack(
        [key_add.reshape(all_tokens, local_width), value_add.reshape(all_tokens, local_width)]
    )
    kv_grads = lax.psum_scatter(kv_part, "blk", scatter_dimension=1, tiled=True)
    grad_queries = query_add.reshape(tok_rows, local_width).astype(jnp.bfloat16)
    grad_keys = kv_grads[0].astype(jnp.bfloat16)
    grad_values = kv_grads[1].astype(jnp.bfloat16)
    dbias_cells = lax.all_to_all(dscores, "col", split_axis=2, concat_axis=0, tiled=True)
    dnormed = jnp.einsum(
        "hij,ch->ijc", dbias_cells, bias_weight, preferred_element_type=jnp.float32
    )
    gain_part = jnp.sum(dnormed * unit, axis=(0, 1))
    weight_part = jnp.einsum("ijc,hij->ch", normed, dbias_cells, preferred_element_type=jnp.float32)
    pair_width = gain_part.shape[0]
    packed = jnp.concatenate([gain_part, weight_part.reshape(-1)])
    packed = jnp.sum(lax.all_gather(lax.psum(packed, "col"), "blk"), axis=0)
    grad_gain = packed[:pair_width]
    grad_weight = packed[pair_width:].reshape(weight_part.shape)
    scaled = dnormed * norm_gain
    grad_pair = (
        inverse
        * (
            scaled
            - jnp.mean(scaled, axis=-1, keepdims=True)
            - unit * jnp.mean(scaled * unit, axis=-1, keepdims=True)
        )
    ).astype(jnp.bfloat16)
    return (grad_queries, grad_keys, grad_values, grad_pair, grad_gain, grad_weight)


def solution(mesh):
    placed = (
        P("blk", "col"),
        P("blk", "col"),
        P("blk", "col"),
        P("blk", "col"),
        P("blk", "col", None),
        P(),
        P(),
        P(),
        P(),
    )
    return jax.shard_map(
        local,
        mesh=mesh,
        in_specs=placed,
        out_specs=(
            P("blk", "col"),
            P("blk", "col"),
            P("blk", "col"),
            P("blk", "col", None),
            P(),
            P(),
        ),
        check_vma=False,
    )
```

```python
import math

import jax
import jax.numpy as jnp
from jax import lax
from jax.experimental import pallas as pl
from jax.experimental.pallas import tpu as pltpu
from jax.sharding import PartitionSpec as P

HEAD_DIM = 24
MASK_BLOCK = 128
ROWS_PER_STEP = 8


def _norm_rows(x, gain):
    centre = jnp.mean(x, axis=-1, keepdims=True)
    shifted = x - centre
    inverse = lax.rsqrt(jnp.mean(shifted * shifted, axis=-1, keepdims=True) + 1e-05)
    unit = shifted * inverse
    return unit, inverse, (unit * gain).astype(jnp.bfloat16)


def _bias_kernel(pair_ref, gain_ref, wt_ref, bias_ref):
    gain = gain_ref[...]
    wt = wt_ref[...]
    for r in range(pair_ref.shape[0]):
        _, _, normed = _norm_rows(pair_ref[r].astype(jnp.float32), gain)
        bias = lax.dot_general(
            wt, normed, (((1,), (1,)), ((), ())), preferred_element_type=jnp.float32
        )
        bias_ref[r] = bias.astype(jnp.bfloat16)


def pair_bias(pair_rep, norm_gain, bias_weight):
    rows, cols, width = pair_rep.shape
    heads = bias_weight.shape[1]
    step = ROWS_PER_STEP
    return pl.pallas_call(
        _bias_kernel,
        out_shape=jax.ShapeDtypeStruct((rows, heads, cols), jnp.bfloat16),
        grid=(rows // step,),
        in_specs=[
            pl.BlockSpec((step, cols, width), lambda i: (i, 0, 0)),
            pl.BlockSpec((1, width), lambda i: (0, 0)),
            pl.BlockSpec((heads, width), lambda i: (0, 0)),
        ],
        out_specs=pl.BlockSpec((step, heads, cols), lambda i: (i, 0, 0)),
        compiler_params=pltpu.CompilerParams(dimension_semantics=("arbitrary",)),
    )(pair_rep, norm_gain.reshape(1, width).astype(jnp.float32), bias_weight.T)


def _grad_kernel(pair_ref, ds_ref, gain_ref, wt_ref, gp_ref, gw_ref, gg_ref):
    @pl.when(pl.program_id(0) == 0)
    def _():
        gw_ref[...] = jnp.zeros_like(gw_ref)
        gg_ref[...] = jnp.zeros_like(gg_ref)

    gain = gain_ref[...]
    wt = wt_ref[...]
    gw = jnp.zeros(gw_ref.shape, jnp.float32)
    gg = jnp.zeros(gg_ref.shape, jnp.float32)
    for r in range(pair_ref.shape[0]):
        unit, inverse, normed = _norm_rows(pair_ref[r].astype(jnp.float32), gain)
        ds = ds_ref[r]
        dnormed = lax.dot_general(
            ds, wt, (((0,), (0,)), ((), ())), preferred_element_type=jnp.float32
        )
        gw = gw + jnp.dot(ds, normed, preferred_element_type=jnp.float32)
        gg = gg + jnp.sum(dnormed * unit, axis=0, keepdims=True)
        scaled = dnormed * gain
        grad = inverse * (
            scaled
            - jnp.mean(scaled, axis=-1, keepdims=True)
            - unit * jnp.mean(scaled * unit, axis=-1, keepdims=True)
        )
        gp_ref[r] = grad.astype(jnp.bfloat16)
    gw_ref[...] += gw
    gg_ref[...] += gg


def pair_grads(pair_rep, dbias, norm_gain, bias_weight):
    rows, cols, width = pair_rep.shape
    heads = bias_weight.shape[1]
    step = ROWS_PER_STEP
    return pl.pallas_call(
        _grad_kernel,
        out_shape=(
            jax.ShapeDtypeStruct((rows, cols, width), jnp.bfloat16),
            jax.ShapeDtypeStruct((heads, width), jnp.float32),
            jax.ShapeDtypeStruct((1, width), jnp.float32),
        ),
        grid=(rows // step,),
        in_specs=[
            pl.BlockSpec((step, cols, width), lambda i: (i, 0, 0)),
            pl.BlockSpec((step, heads, cols), lambda i: (i, 0, 0)),
            pl.BlockSpec((1, width), lambda i: (0, 0)),
            pl.BlockSpec((heads, width), lambda i: (0, 0)),
        ],
        out_specs=(
            pl.BlockSpec((step, cols, width), lambda i: (i, 0, 0)),
            pl.BlockSpec((heads, width), lambda i: (0, 0)),
            pl.BlockSpec((1, width), lambda i: (0, 0)),
        ),
        compiler_params=pltpu.CompilerParams(dimension_semantics=("arbitrary",)),
    )(pair_rep, dbias, norm_gain.reshape(1, width).astype(jnp.float32), bias_weight.T)


def block_onehot(first_token, count, nblocks):
    block_ids = (first_token + jnp.arange(count, dtype=jnp.int32)) // MASK_BLOCK
    return (block_ids[:, None] == jnp.arange(nblocks, dtype=jnp.int32)[None, :]).astype(
        jnp.bfloat16
    )


def local(
    queries, key_proj, value_proj, out_grad, pair_rep, norm_gain, bias_weight, chain_ids, block_mask
):
    tok_rows = queries.shape[0]
    local_width = queries.shape[1]
    local_heads = local_width // HEAD_DIM
    scale_factor = 1.0 / math.sqrt(HEAD_DIM)
    blk_index = lax.axis_index("blk")
    blk_count = lax.axis_size("blk")
    all_tokens = blk_count * tok_rows
    row_start = blk_index * tok_rows
    nblocks = block_mask.shape[0]
    rows_table = jnp.dot(
        block_onehot(row_start, tok_rows, nblocks),
        block_mask.astype(jnp.bfloat16),
        preferred_element_type=jnp.float32,
    ).astype(jnp.bfloat16)
    chain_rows = lax.dynamic_slice_in_dim(chain_ids, row_start, tok_rows)
    hits = lax.dot_general(
        rows_table,
        block_onehot(0, all_tokens, nblocks),
        (((1,), (1,)), ((), ())),
        preferred_element_type=jnp.float32,
    )
    allowed = (hits > 0.5) | (chain_rows[:, None] == chain_ids[None, :])

    kv_local = jnp.stack([key_proj, value_proj])
    kv_rep = jnp.broadcast_to(kv_local[None], (blk_count,) + kv_local.shape)
    kv_all = lax.all_to_all(kv_rep, "blk", split_axis=0, concat_axis=0, tiled=True)
    kv_all = jnp.transpose(kv_all, (1, 0, 2, 3)).reshape(2, all_tokens, local_width)
    query_heads = queries.reshape(tok_rows, local_heads, HEAD_DIM)
    grad_heads = out_grad.reshape(tok_rows, local_heads, HEAD_DIM)
    key_heads = kv_all[0].reshape(all_tokens, local_heads, HEAD_DIM)
    value_heads = kv_all[1].reshape(all_tokens, local_heads, HEAD_DIM)
    bias_local = pair_bias(pair_rep, norm_gain, bias_weight)
    bias_mine = lax.all_to_all(bias_local, "col", split_axis=1, concat_axis=2, tiled=True)
    bias_mine = jnp.transpose(bias_mine, (1, 0, 2))

    scores = (
        jnp.einsum("qhd,khd->hqk", query_heads, key_heads, preferred_element_type=jnp.float32)
        * scale_factor
        + bias_mine.astype(jnp.float32)
    )
    masked = jnp.where(allowed[None], scores, -jnp.inf)
    row_top = jnp.max(masked, axis=-1, keepdims=True)
    expo = jnp.where(allowed[None], jnp.exp(scores - row_top), 0.0)
    totals = jnp.sum(expo, axis=-1, keepdims=True)
    log_total = row_top + jnp.log(totals)
    weights = jnp.where(allowed[None], jnp.exp(scores - log_total), 0.0)
    probs = weights.astype(jnp.bfloat16)
    attended = jnp.einsum("hqk,khd->qhd", weights, value_heads.astype(jnp.float32))
    delta = jnp.sum(grad_heads.astype(jnp.float32) * attended, axis=-1).T
    dprobs = jnp.einsum(
        "qhd,khd->hqk", grad_heads, value_heads, preferred_element_type=jnp.float32
    )
    dscores = (probs.astype(jnp.float32) * (dprobs - delta[:, :, None])).astype(jnp.bfloat16)
    query_add = (
        jnp.einsum("hqk,khd->qhd", dscores, key_heads, preferred_element_type=jnp.float32)
        * scale_factor
    )
    key_add = (
        jnp.einsum("hqk,qhd->khd", dscores, query_heads, preferred_element_type=jnp.float32)
        * scale_factor
    )
    value_add = jnp.einsum("hqk,qhd->khd", probs, grad_heads, preferred_element_type=jnp.float32)
    kv_part = jnp.stack(
        [key_add.reshape(all_tokens, local_width), value_add.reshape(all_tokens, local_width)]
    )
    kv_grads = lax.psum_scatter(kv_part, "blk", scatter_dimension=1, tiled=True)
    grad_queries = query_add.reshape(tok_rows, local_width).astype(jnp.bfloat16)
    grad_keys = kv_grads[0].astype(jnp.bfloat16)
    grad_values = kv_grads[1].astype(jnp.bfloat16)
    dbias_cells = lax.all_to_all(
        jnp.transpose(dscores, (1, 0, 2)), "col", split_axis=2, concat_axis=1, tiled=True
    )
    grad_pair, weight_part, gain_part = pair_grads(pair_rep, dbias_cells, norm_gain, bias_weight)
    pair_width = gain_part.shape[1]
    packed = jnp.concatenate([gain_part[0], weight_part.T.reshape(-1)])
    packed = jnp.sum(lax.all_gather(lax.psum(packed, "col"), "blk"), axis=0)
    grad_gain = packed[:pair_width]
    grad_weight = packed[pair_width:].reshape(weight_part.shape[::-1])
    return (grad_queries, grad_keys, grad_values, grad_pair, grad_gain, grad_weight)


def solution(mesh):
    placed = (
        P("blk", "col"),
        P("blk", "col"),
        P("blk", "col"),
        P("blk", "col"),
        P("blk", "col", None),
        P(),
        P(),
        P(),
        P(),
    )
    return jax.shard_map(
        local,
        mesh=mesh,
        in_specs=placed,
        out_specs=(
            P("blk", "col"),
            P("blk", "col"),
            P("blk", "col"),
            P("blk", "col", None),
            P(),
            P(),
        ),
        check_vma=False,
    )
```

```python
import math

import jax
import jax.numpy as jnp
from jax import lax
from jax.experimental import pallas as pl
from jax.experimental.pallas import tpu as pltpu
from jax.sharding import PartitionSpec as P

HEAD_DIM = 24
MASK_BLOCK = 128
ROWS_PER_STEP = 8
CHUNKS = 1


def _norm_rows(x, gain):
    centre = jnp.mean(x, axis=-1, keepdims=True)
    shifted = x - centre
    inverse = lax.rsqrt(jnp.mean(shifted * shifted, axis=-1, keepdims=True) + 1e-05)
    unit = shifted * inverse
    return unit, inverse, (unit * gain).astype(jnp.bfloat16)


def _bias_kernel(pair_ref, gain_ref, wt_ref, bias_ref):
    gain = gain_ref[...]
    wt = wt_ref[...]
    for r in range(pair_ref.shape[0]):
        _, _, normed = _norm_rows(pair_ref[r].astype(jnp.float32), gain)
        bias = lax.dot_general(
            wt, normed, (((1,), (1,)), ((), ())), preferred_element_type=jnp.float32
        )
        bias_ref[r] = bias.astype(jnp.bfloat16)


def pair_bias(pair_rep, norm_gain, bias_weight, first, count):
    _, cols, width = pair_rep.shape
    heads = bias_weight.shape[1]
    step = ROWS_PER_STEP
    base = first // step
    return pl.pallas_call(
        _bias_kernel,
        out_shape=jax.ShapeDtypeStruct((count, heads, cols), jnp.bfloat16),
        grid=(count // step,),
        in_specs=[
            pl.BlockSpec((step, cols, width), lambda i: (i + base, 0, 0)),
            pl.BlockSpec((1, width), lambda i: (0, 0)),
            pl.BlockSpec((heads, width), lambda i: (0, 0)),
        ],
        out_specs=pl.BlockSpec((step, heads, cols), lambda i: (i, 0, 0)),
        compiler_params=pltpu.CompilerParams(dimension_semantics=("arbitrary",)),
    )(pair_rep, norm_gain.reshape(1, width).astype(jnp.float32), bias_weight.T)


def _grad_kernel(pair_ref, ds_ref, gain_ref, wt_ref, *refs):
    gp_ref, gw_ref, gg_ref = refs[-3:]

    @pl.when(pl.program_id(0) == 0)
    def _():
        gw_ref[...] = jnp.zeros_like(gw_ref)
        gg_ref[...] = jnp.zeros_like(gg_ref)

    gain = gain_ref[...]
    wt = wt_ref[...]
    gw = jnp.zeros(gw_ref.shape, jnp.float32)
    gg = jnp.zeros(gg_ref.shape, jnp.float32)
    for r in range(pair_ref.shape[0]):
        unit, inverse, normed = _norm_rows(pair_ref[r].astype(jnp.float32), gain)
        ds = ds_ref[r]
        ds_t = ds.astype(jnp.float32).T.astype(jnp.bfloat16)
        dnormed = jnp.dot(ds_t, wt, preferred_element_type=jnp.float32)
        gw = gw + jnp.dot(ds, normed, preferred_element_type=jnp.float32)
        gg = gg + jnp.sum(dnormed * unit, axis=0, keepdims=True)
        scaled = dnormed * gain
        grad = inverse * (
            scaled
            - jnp.mean(scaled, axis=-1, keepdims=True)
            - unit * jnp.mean(scaled * unit, axis=-1, keepdims=True)
        )
        gp_ref[r] = grad.astype(jnp.bfloat16)
    gw_ref[...] += gw
    gg_ref[...] += gg


def pair_grads(pair_rep, dbias, norm_gain, bias_weight, first, into):
    rows, cols, width = pair_rep.shape
    count = dbias.shape[0]
    heads = bias_weight.shape[1]
    step = ROWS_PER_STEP
    base = first // step
    operands = [pair_rep, dbias, norm_gain.reshape(1, width).astype(jnp.float32), bias_weight.T]
    in_specs = [
        pl.BlockSpec((step, cols, width), lambda i: (i + base, 0, 0)),
        pl.BlockSpec((step, heads, cols), lambda i: (i, 0, 0)),
        pl.BlockSpec((1, width), lambda i: (0, 0)),
        pl.BlockSpec((heads, width), lambda i: (0, 0)),
    ]
    aliases = {}
    if into is not None:
        aliases = {len(operands): 0}
        operands.append(into)
        in_specs.append(pl.BlockSpec(memory_space=pl.ANY))
    return pl.pallas_call(
        _grad_kernel,
        out_shape=(
            jax.ShapeDtypeStruct((rows, cols, width), jnp.bfloat16),
            jax.ShapeDtypeStruct((heads, width), jnp.float32),
            jax.ShapeDtypeStruct((1, width), jnp.float32),
        ),
        grid=(count // step,),
        in_specs=in_specs,
        out_specs=(
            pl.BlockSpec((step, cols, width), lambda i: (i + base, 0, 0)),
            pl.BlockSpec((heads, width), lambda i: (0, 0)),
            pl.BlockSpec((1, width), lambda i: (0, 0)),
        ),
        input_output_aliases=aliases,
        compiler_params=pltpu.CompilerParams(dimension_semantics=("arbitrary",)),
    )(*operands)


def block_onehot(first_token, count, nblocks):
    block_ids = (first_token + jnp.arange(count, dtype=jnp.int32)) // MASK_BLOCK
    return (block_ids[:, None] == jnp.arange(nblocks, dtype=jnp.int32)[None, :]).astype(
        jnp.bfloat16
    )


def local(
    queries, key_proj, value_proj, out_grad, pair_rep, norm_gain, bias_weight, chain_ids, block_mask
):
    tok_rows = queries.shape[0]
    local_width = queries.shape[1]
    local_heads = local_width // HEAD_DIM
    scale_factor = 1.0 / math.sqrt(HEAD_DIM)
    blk_index = lax.axis_index("blk")
    blk_count = lax.axis_size("blk")
    all_tokens = blk_count * tok_rows
    row_start = blk_index * tok_rows
    nblocks = block_mask.shape[0]
    count = tok_rows // CHUNKS
    firsts = [c * count for c in range(CHUNKS)]

    kv_local = jnp.stack([key_proj, value_proj])
    kv_rep = jnp.broadcast_to(kv_local[None], (blk_count,) + kv_local.shape)
    kv_all = lax.all_to_all(kv_rep, "blk", split_axis=0, concat_axis=0, tiled=True)
    kv_all = jnp.transpose(kv_all, (1, 0, 2, 3)).reshape(2, all_tokens, local_width)
    key_heads = kv_all[0].reshape(all_tokens, local_heads, HEAD_DIM)
    value_heads = kv_all[1].reshape(all_tokens, local_heads, HEAD_DIM)

    bias_parts = []
    for first in firsts:
        bias_local = pair_bias(pair_rep, norm_gain, bias_weight, first, count)
        bias_mine = lax.all_to_all(bias_local, "col", split_axis=1, concat_axis=2, tiled=True)
        bias_parts.append(jnp.transpose(bias_mine, (1, 0, 2)))

    column_table = block_onehot(0, all_tokens, nblocks)
    query_grads, kv_parts, dbias_parts = [], [], []
    for first, bias_mine in zip(firsts, bias_parts):
        rows_table = jnp.dot(
            block_onehot(row_start + first, count, nblocks),
            block_mask.astype(jnp.bfloat16),
            preferred_element_type=jnp.float32,
        ).astype(jnp.bfloat16)
        chain_rows = lax.dynamic_slice_in_dim(chain_ids, row_start + first, count)
        hits = lax.dot_general(
            rows_table, column_table, (((1,), (1,)), ((), ())), preferred_element_type=jnp.float32
        )
        allowed = (hits > 0.5) | (chain_rows[:, None] == chain_ids[None, :])
        query_heads = queries[first : first + count].reshape(count, local_heads, HEAD_DIM)
        grad_heads = out_grad[first : first + count].reshape(count, local_heads, HEAD_DIM)

        scores = (
            jnp.einsum("qhd,khd->hqk", query_heads, key_heads, preferred_element_type=jnp.float32)
            * scale_factor
            + bias_mine.astype(jnp.float32)
        )
        masked = jnp.where(allowed[None], scores, -jnp.inf)
        row_top = jnp.max(masked, axis=-1, keepdims=True)
        expo = jnp.where(allowed[None], jnp.exp(scores - row_top), 0.0)
        totals = jnp.sum(expo, axis=-1, keepdims=True)
        log_total = row_top + jnp.log(totals)
        weights = jnp.where(allowed[None], jnp.exp(scores - log_total), 0.0)
        probs = weights.astype(jnp.bfloat16)
        attended = jnp.einsum("hqk,khd->qhd", weights, value_heads.astype(jnp.float32))
        delta = jnp.sum(grad_heads.astype(jnp.float32) * attended, axis=-1).T
        dprobs = jnp.einsum(
            "qhd,khd->hqk", grad_heads, value_heads, preferred_element_type=jnp.float32
        )
        dscores = (probs.astype(jnp.float32) * (dprobs - delta[:, :, None])).astype(jnp.bfloat16)
        dbias_parts.append(
            lax.all_to_all(
                jnp.transpose(dscores, (1, 0, 2)), "col", split_axis=2, concat_axis=1, tiled=True
            )
        )
        query_grads.append(
            jnp.einsum("hqk,khd->qhd", dscores, key_heads, preferred_element_type=jnp.float32)
            * scale_factor
        )
        key_add = (
            jnp.einsum("hqk,qhd->khd", dscores, query_heads, preferred_element_type=jnp.float32)
            * scale_factor
        )
        value_add = jnp.einsum(
            "hqk,qhd->khd", probs, grad_heads, preferred_element_type=jnp.float32
        )
        kv_parts.append(
            jnp.stack(
                [key_add.reshape(all_tokens, local_width), value_add.reshape(all_tokens, local_width)]
            )
        )
    kv_part = kv_parts[0]
    for extra in kv_parts[1:]:
        kv_part = kv_part + extra
    kv_grads = lax.psum_scatter(kv_part, "blk", scatter_dimension=1, tiled=True)
    grad_queries = jnp.concatenate(query_grads, axis=0).reshape(tok_rows, local_width)
    grad_queries = grad_queries.astype(jnp.bfloat16)
    grad_keys = kv_grads[0].astype(jnp.bfloat16)
    grad_values = kv_grads[1].astype(jnp.bfloat16)

    grad_pair = None
    weight_part = 0.0
    gain_part = 0.0
    for first, dbias_cells in zip(firsts, dbias_parts):
        grad_pair, weight_add, gain_add = pair_grads(
            pair_rep, dbias_cells, norm_gain, bias_weight, first, grad_pair
        )
        weight_part = weight_part + weight_add
        gain_part = gain_part + gain_add
    pair_width = gain_part.shape[1]
    packed = jnp.concatenate([gain_part[0], weight_part.T.reshape(-1)])
    packed = jnp.sum(lax.all_gather(lax.psum(packed, "col"), "blk"), axis=0)
    grad_gain = packed[:pair_width]
    grad_weight = packed[pair_width:].reshape(weight_part.shape[::-1])
    return (grad_queries, grad_keys, grad_values, grad_pair, grad_gain, grad_weight)


def solution(mesh):
    placed = (
        P("blk", "col"),
        P("blk", "col"),
        P("blk", "col"),
        P("blk", "col"),
        P("blk", "col", None),
        P(),
        P(),
        P(),
        P(),
    )
    return jax.shard_map(
        local,
        mesh=mesh,
        in_specs=placed,
        out_specs=(
            P("blk", "col"),
            P("blk", "col"),
            P("blk", "col"),
            P("blk", "col", None),
            P(),
            P(),
        ),
        check_vma=False,
    )
```

```python
import math

import jax
import jax.numpy as jnp
from jax import lax
from jax.experimental import pallas as pl
from jax.experimental.pallas import tpu as pltpu
from jax.sharding import PartitionSpec as P

HEAD_DIM = 24
MASK_BLOCK = 128
ROWS_PER_STEP = 16
CHUNKS = 1


def _norm_rows(x, gain):
    centre = jnp.mean(x, axis=-1, keepdims=True)
    shifted = x - centre
    inverse = lax.rsqrt(jnp.mean(shifted * shifted, axis=-1, keepdims=True) + 1e-05)
    unit = shifted * inverse
    return unit, inverse, (unit * gain).astype(jnp.bfloat16)


def _bias_kernel(pair_ref, gain_ref, wt_ref, bias_ref):
    gain = gain_ref[...]
    wt = wt_ref[...]
    for r in range(pair_ref.shape[0]):
        _, _, normed = _norm_rows(pair_ref[r].astype(jnp.float32), gain)
        bias = lax.dot_general(
            wt, normed, (((1,), (1,)), ((), ())), preferred_element_type=jnp.float32
        )
        bias_ref[:, r, :] = bias.astype(jnp.bfloat16)


def pair_bias(pair_rep, norm_gain, bias_weight, first, count):
    _, cols, width = pair_rep.shape
    heads = bias_weight.shape[1]
    step = ROWS_PER_STEP
    base = first // step
    return pl.pallas_call(
        _bias_kernel,
        out_shape=jax.ShapeDtypeStruct((heads, count, cols), jnp.bfloat16),
        grid=(count // step,),
        in_specs=[
            pl.BlockSpec((step, cols, width), lambda i: (i + base, 0, 0)),
            pl.BlockSpec((1, width), lambda i: (0, 0)),
            pl.BlockSpec((heads, width), lambda i: (0, 0)),
        ],
        out_specs=pl.BlockSpec((heads, step, cols), lambda i: (0, i, 0)),
        compiler_params=pltpu.CompilerParams(dimension_semantics=("arbitrary",)),
    )(pair_rep, norm_gain.reshape(1, width).astype(jnp.float32), bias_weight.T)


def _grad_kernel(pair_ref, ds_ref, gain_ref, wt_ref, *refs):
    gp_ref, gw_ref, gg_ref = refs[-3:]

    @pl.when(pl.program_id(0) == 0)
    def _():
        gw_ref[...] = jnp.zeros_like(gw_ref)
        gg_ref[...] = jnp.zeros_like(gg_ref)

    gain = gain_ref[...]
    wt = wt_ref[...]
    gw = jnp.zeros(gw_ref.shape, jnp.float32)
    gg = jnp.zeros(gg_ref.shape, jnp.float32)
    for r in range(pair_ref.shape[0]):
        unit, inverse, normed = _norm_rows(pair_ref[r].astype(jnp.float32), gain)
        ds = ds_ref[:, r, :]
        ds_t = ds.astype(jnp.float32).T.astype(jnp.bfloat16)
        dnormed = jnp.dot(ds_t, wt, preferred_element_type=jnp.float32)
        gw = gw + jnp.dot(ds, normed, preferred_element_type=jnp.float32)
        gg = gg + jnp.sum(dnormed * unit, axis=0, keepdims=True)
        scaled = dnormed * gain
        grad = inverse * (
            scaled
            - jnp.mean(scaled, axis=-1, keepdims=True)
            - unit * jnp.mean(scaled * unit, axis=-1, keepdims=True)
        )
        gp_ref[r] = grad.astype(jnp.bfloat16)
    gw_ref[...] += gw
    gg_ref[...] += gg


def pair_grads(pair_rep, dbias, norm_gain, bias_weight, first, into):
    rows, cols, width = pair_rep.shape
    count = dbias.shape[1]
    heads = bias_weight.shape[1]
    step = ROWS_PER_STEP
    base = first // step
    operands = [pair_rep, dbias, norm_gain.reshape(1, width).astype(jnp.float32), bias_weight.T]
    in_specs = [
        pl.BlockSpec((step, cols, width), lambda i: (i + base, 0, 0)),
        pl.BlockSpec((heads, step, cols), lambda i: (0, i, 0)),
        pl.BlockSpec((1, width), lambda i: (0, 0)),
        pl.BlockSpec((heads, width), lambda i: (0, 0)),
    ]
    aliases = {}
    if into is not None:
        aliases = {len(operands): 0}
        operands.append(into)
        in_specs.append(pl.BlockSpec(memory_space=pl.ANY))
    return pl.pallas_call(
        _grad_kernel,
        out_shape=(
            jax.ShapeDtypeStruct((rows, cols, width), jnp.bfloat16),
            jax.ShapeDtypeStruct((heads, width), jnp.float32),
            jax.ShapeDtypeStruct((1, width), jnp.float32),
        ),
        grid=(count // step,),
        in_specs=in_specs,
        out_specs=(
            pl.BlockSpec((step, cols, width), lambda i: (i + base, 0, 0)),
            pl.BlockSpec((heads, width), lambda i: (0, 0)),
            pl.BlockSpec((1, width), lambda i: (0, 0)),
        ),
        input_output_aliases=aliases,
        compiler_params=pltpu.CompilerParams(dimension_semantics=("arbitrary",)),
    )(*operands)


def block_onehot(first_token, count, nblocks):
    block_ids = (first_token + jnp.arange(count, dtype=jnp.int32)) // MASK_BLOCK
    return (block_ids[:, None] == jnp.arange(nblocks, dtype=jnp.int32)[None, :]).astype(
        jnp.bfloat16
    )


def local(
    queries, key_proj, value_proj, out_grad, pair_rep, norm_gain, bias_weight, chain_ids, block_mask
):
    tok_rows = queries.shape[0]
    local_width = queries.shape[1]
    local_heads = local_width // HEAD_DIM
    scale_factor = 1.0 / math.sqrt(HEAD_DIM)
    blk_index = lax.axis_index("blk")
    blk_count = lax.axis_size("blk")
    all_tokens = blk_count * tok_rows
    row_start = blk_index * tok_rows
    nblocks = block_mask.shape[0]
    count = tok_rows // CHUNKS
    firsts = [c * count for c in range(CHUNKS)]

    kv_local = jnp.stack([key_proj, value_proj])
    kv_rep = jnp.broadcast_to(kv_local[None], (blk_count,) + kv_local.shape)
    kv_all = lax.all_to_all(kv_rep, "blk", split_axis=0, concat_axis=0, tiled=True)
    kv_all = jnp.transpose(kv_all, (1, 0, 2, 3)).reshape(2, all_tokens, local_width)
    key_heads = kv_all[0].reshape(all_tokens, local_heads, HEAD_DIM)
    value_heads = kv_all[1].reshape(all_tokens, local_heads, HEAD_DIM)

    bias_parts = []
    for first in firsts:
        bias_local = pair_bias(pair_rep, norm_gain, bias_weight, first, count)
        heads, _, cols = bias_local.shape
        groups = lax.axis_size("col")
        bias_mine = lax.all_to_all(
            bias_local.reshape(groups, heads // groups, count, cols),
            "col", split_axis=0, concat_axis=0, tiled=True,
        )
        bias_mine = jnp.transpose(bias_mine, (1, 2, 0, 3)).reshape(local_heads, count, all_tokens)
        bias_parts.append(bias_mine)

    column_table = block_onehot(0, all_tokens, nblocks)
    query_grads, kv_parts, dbias_parts = [], [], []
    for first, bias_mine in zip(firsts, bias_parts):
        rows_table = jnp.dot(
            block_onehot(row_start + first, count, nblocks),
            block_mask.astype(jnp.bfloat16),
            preferred_element_type=jnp.float32,
        ).astype(jnp.bfloat16)
        chain_rows = lax.dynamic_slice_in_dim(chain_ids, row_start + first, count)
        hits = lax.dot_general(
            rows_table, column_table, (((1,), (1,)), ((), ())), preferred_element_type=jnp.float32
        )
        allowed = (hits > 0.5) | (chain_rows[:, None] == chain_ids[None, :])
        query_heads = queries[first : first + count].reshape(count, local_heads, HEAD_DIM)
        grad_heads = out_grad[first : first + count].reshape(count, local_heads, HEAD_DIM)

        scores = (
            jnp.einsum("qhd,khd->hqk", query_heads, key_heads, preferred_element_type=jnp.float32)
            * scale_factor
            + bias_mine.astype(jnp.float32)
        )
        masked = jnp.where(allowed[None], scores, -jnp.inf)
        row_top = jnp.max(masked, axis=-1, keepdims=True)
        expo = jnp.where(allowed[None], jnp.exp(scores - row_top), 0.0)
        totals = jnp.sum(expo, axis=-1, keepdims=True)
        log_total = row_top + jnp.log(totals)
        weights = jnp.where(allowed[None], jnp.exp(scores - log_total), 0.0)
        probs = weights.astype(jnp.bfloat16)
        attended = jnp.einsum("hqk,khd->qhd", weights, value_heads.astype(jnp.float32))
        delta = jnp.sum(grad_heads.astype(jnp.float32) * attended, axis=-1).T
        dprobs = jnp.einsum(
            "qhd,khd->hqk", grad_heads, value_heads, preferred_element_type=jnp.float32
        )
        dscores = (probs.astype(jnp.float32) * (dprobs - delta[:, :, None])).astype(jnp.bfloat16)
        groups = lax.axis_size("col")
        dscores_blocks = jnp.transpose(
            dscores.reshape(local_heads, count, groups, all_tokens // groups), (2, 0, 1, 3)
        )
        dbias_cells = lax.all_to_all(dscores_blocks, "col", split_axis=0, concat_axis=0, tiled=True)
        dbias_parts.append(dbias_cells.reshape(groups * local_heads, count, all_tokens // groups))
        query_grads.append(
            jnp.einsum("hqk,khd->qhd", dscores, key_heads, preferred_element_type=jnp.float32)
            * scale_factor
        )
        key_add = (
            jnp.einsum("hqk,qhd->khd", dscores, query_heads, preferred_element_type=jnp.float32)
            * scale_factor
        )
        value_add = jnp.einsum(
            "hqk,qhd->khd", probs, grad_heads, preferred_element_type=jnp.float32
        )
        kv_parts.append(
            jnp.stack(
                [key_add.reshape(all_tokens, local_width), value_add.reshape(all_tokens, local_width)]
            )
        )
    kv_part = kv_parts[0]
    for extra in kv_parts[1:]:
        kv_part = kv_part + extra
    kv_grads = lax.psum_scatter(kv_part, "blk", scatter_dimension=1, tiled=True)
    grad_queries = jnp.concatenate(query_grads, axis=0).reshape(tok_rows, local_width)
    grad_queries = grad_queries.astype(jnp.bfloat16)
    grad_keys = kv_grads[0].astype(jnp.bfloat16)
    grad_values = kv_grads[1].astype(jnp.bfloat16)

    grad_pair = None
    weight_part = 0.0
    gain_part = 0.0
    for first, dbias_cells in zip(firsts, dbias_parts):
        grad_pair, weight_add, gain_add = pair_grads(
            pair_rep, dbias_cells, norm_gain, bias_weight, first, grad_pair
        )
        weight_part = weight_part + weight_add
        gain_part = gain_part + gain_add
    pair_width = gain_part.shape[1]
    packed = jnp.concatenate([gain_part[0], weight_part.T.reshape(-1)])
    packed = jnp.sum(lax.all_gather(lax.psum(packed, "col"), "blk"), axis=0)
    grad_gain = packed[:pair_width]
    grad_weight = packed[pair_width:].reshape(weight_part.shape[::-1])
    return (grad_queries, grad_keys, grad_values, grad_pair, grad_gain, grad_weight)


def solution(mesh):
    placed = (
        P("blk", "col"),
        P("blk", "col"),
        P("blk", "col"),
        P("blk", "col"),
        P("blk", "col", None),
        P(),
        P(),
        P(),
        P(),
    )
    return jax.shard_map(
        local,
        mesh=mesh,
        in_specs=placed,
        out_specs=(
            P("blk", "col"),
            P("blk", "col"),
            P("blk", "col"),
            P("blk", "col", None),
            P(),
            P(),
        ),
        check_vma=False,
    )
```

```python
import math

import jax
import jax.numpy as jnp
from jax import lax
from jax.experimental import pallas as pl
from jax.experimental.pallas import tpu as pltpu
from jax.sharding import PartitionSpec as P

HEAD_DIM = 24
MASK_BLOCK = 128
ROWS_PER_STEP = 16
CHUNKS = 1


def _norm_rows(x, gain):
    centre = jnp.mean(x, axis=-1, keepdims=True)
    shifted = x - centre
    inverse = lax.rsqrt(jnp.mean(shifted * shifted, axis=-1, keepdims=True) + 1e-05)
    unit = shifted * inverse
    return unit, inverse, (unit * gain).astype(jnp.bfloat16)


def _bias_kernel(pair_ref, gain_ref, wt_ref, bias_ref):
    gain = gain_ref[...]
    wt = wt_ref[...]
    for r in range(pair_ref.shape[0]):
        _, _, normed = _norm_rows(pair_ref[r].astype(jnp.float32), gain)
        bias = lax.dot_general(
            wt, normed, (((1,), (1,)), ((), ())), preferred_element_type=jnp.float32
        )
        bias_ref[:, r, :] = bias.astype(jnp.bfloat16)


def pair_bias(pair_rep, norm_gain, bias_weight, first, count):
    _, cols, width = pair_rep.shape
    heads = bias_weight.shape[1]
    step = ROWS_PER_STEP
    base = first // step
    return pl.pallas_call(
        _bias_kernel,
        out_shape=jax.ShapeDtypeStruct((heads, count, cols), jnp.bfloat16),
        grid=(count // step,),
        in_specs=[
            pl.BlockSpec((step, cols, width), lambda i: (i + base, 0, 0)),
            pl.BlockSpec((1, width), lambda i: (0, 0)),
            pl.BlockSpec((heads, width), lambda i: (0, 0)),
        ],
        out_specs=pl.BlockSpec((heads, step, cols), lambda i: (0, i, 0)),
        compiler_params=pltpu.CompilerParams(dimension_semantics=("arbitrary",)),
    )(pair_rep, norm_gain.reshape(1, width).astype(jnp.float32), bias_weight.T)


def _grad_kernel(pair_ref, ds_ref, gain_ref, wt_ref, *refs):
    gp_ref, gw_ref, gg_ref = refs[-3:]

    @pl.when(pl.program_id(0) == 0)
    def _():
        gw_ref[...] = jnp.zeros_like(gw_ref)
        gg_ref[...] = jnp.zeros_like(gg_ref)

    gain = gain_ref[...]
    wt = wt_ref[...]
    gw = jnp.zeros(gw_ref.shape, jnp.float32)
    gg = jnp.zeros(gg_ref.shape, jnp.float32)
    for r in range(pair_ref.shape[0]):
        unit, inverse, normed = _norm_rows(pair_ref[r].astype(jnp.float32), gain)
        ds = ds_ref[:, r, :]
        ds_t = ds.astype(jnp.float32).T.astype(jnp.bfloat16)
        dnormed = jnp.dot(ds_t, wt, preferred_element_type=jnp.float32)
        gw = gw + jnp.dot(ds, normed, preferred_element_type=jnp.float32)
        gg = gg + jnp.sum(dnormed * unit, axis=0, keepdims=True)
        scaled = dnormed * gain
        grad = inverse * (
            scaled
            - jnp.mean(scaled, axis=-1, keepdims=True)
            - unit * jnp.mean(scaled * unit, axis=-1, keepdims=True)
        )
        gp_ref[r] = grad.astype(jnp.bfloat16)
    gw_ref[...] += gw
    gg_ref[...] += gg


def pair_grads(pair_rep, dbias, norm_gain, bias_weight, first, into):
    rows, cols, width = pair_rep.shape
    count = dbias.shape[1]
    heads = bias_weight.shape[1]
    step = ROWS_PER_STEP
    base = first // step
    operands = [pair_rep, dbias, norm_gain.reshape(1, width).astype(jnp.float32), bias_weight.T]
    in_specs = [
        pl.BlockSpec((step, cols, width), lambda i: (i + base, 0, 0)),
        pl.BlockSpec((heads, step, cols), lambda i: (0, i, 0)),
        pl.BlockSpec((1, width), lambda i: (0, 0)),
        pl.BlockSpec((heads, width), lambda i: (0, 0)),
    ]
    aliases = {}
    if into is not None:
        aliases = {len(operands): 0}
        operands.append(into)
        in_specs.append(pl.BlockSpec(memory_space=pl.ANY))
    return pl.pallas_call(
        _grad_kernel,
        out_shape=(
            jax.ShapeDtypeStruct((rows, cols, width), jnp.bfloat16),
            jax.ShapeDtypeStruct((heads, width), jnp.float32),
            jax.ShapeDtypeStruct((1, width), jnp.float32),
        ),
        grid=(count // step,),
        in_specs=in_specs,
        out_specs=(
            pl.BlockSpec((step, cols, width), lambda i: (i + base, 0, 0)),
            pl.BlockSpec((heads, width), lambda i: (0, 0)),
            pl.BlockSpec((1, width), lambda i: (0, 0)),
        ),
        input_output_aliases=aliases,
        compiler_params=pltpu.CompilerParams(dimension_semantics=("arbitrary",)),
    )(*operands)


def block_onehot(first_token, count, nblocks):
    block_ids = (first_token + jnp.arange(count, dtype=jnp.int32)) // MASK_BLOCK
    return (block_ids[:, None] == jnp.arange(nblocks, dtype=jnp.int32)[None, :]).astype(
        jnp.bfloat16
    )


def local(
    queries, key_proj, value_proj, out_grad, pair_rep, norm_gain, bias_weight, chain_ids, block_mask
):
    tok_rows = queries.shape[0]
    local_width = queries.shape[1]
    local_heads = local_width // HEAD_DIM
    scale_factor = 1.0 / math.sqrt(HEAD_DIM)
    blk_index = lax.axis_index("blk")
    blk_count = lax.axis_size("blk")
    all_tokens = blk_count * tok_rows
    row_start = blk_index * tok_rows
    nblocks = block_mask.shape[0]
    count = tok_rows // CHUNKS
    firsts = [c * count for c in range(CHUNKS)]

    kv_local = jnp.stack([key_proj, value_proj])
    kv_rep = jnp.broadcast_to(kv_local[None], (blk_count,) + kv_local.shape)
    kv_all = lax.all_to_all(kv_rep, "blk", split_axis=0, concat_axis=0, tiled=True)
    kv_all = jnp.transpose(kv_all, (1, 0, 2, 3)).reshape(2, all_tokens, local_width)
    key_heads = kv_all[0].reshape(all_tokens, local_heads, HEAD_DIM)
    value_heads = kv_all[1].reshape(all_tokens, local_heads, HEAD_DIM)

    bias_parts = []
    for first in firsts:
        bias_local = pair_bias(pair_rep, norm_gain, bias_weight, first, count)
        heads, _, cols = bias_local.shape
        groups = lax.axis_size("col")
        bias_mine = lax.all_to_all(
            bias_local.reshape(groups, heads // groups, count, cols),
            "col", split_axis=0, concat_axis=0, tiled=True,
        )
        bias_mine = jnp.transpose(bias_mine, (1, 2, 0, 3)).reshape(local_heads, count, all_tokens)
        bias_parts.append(bias_mine)

    column_table = block_onehot(0, all_tokens, nblocks)
    query_grads, kv_parts, dbias_parts = [], [], []
    for first, bias_mine in zip(firsts, bias_parts):
        rows_table = jnp.dot(
            block_onehot(row_start + first, count, nblocks),
            block_mask.astype(jnp.bfloat16),
            preferred_element_type=jnp.float32,
        ).astype(jnp.bfloat16)
        chain_rows = lax.dynamic_slice_in_dim(chain_ids, row_start + first, count)
        hits = lax.dot_general(
            rows_table, column_table, (((1,), (1,)), ((), ())), preferred_element_type=jnp.float32
        )
        allowed = (hits > 0.5) | (chain_rows[:, None] == chain_ids[None, :])
        query_heads = queries[first : first + count].reshape(count, local_heads, HEAD_DIM)
        grad_heads = out_grad[first : first + count].reshape(count, local_heads, HEAD_DIM)

        scores = (
            jnp.einsum("qhd,khd->hqk", query_heads, key_heads, preferred_element_type=jnp.float32)
            * scale_factor
            + bias_mine.astype(jnp.float32)
        )
        masked = jnp.where(allowed[None], scores, -jnp.inf)
        row_top = jnp.max(masked, axis=-1, keepdims=True)
        expo = jnp.where(allowed[None], jnp.exp(scores - row_top), 0.0)
        totals = jnp.sum(expo, axis=-1, keepdims=True)
        log_total = row_top + jnp.log(totals)
        weights = jnp.where(allowed[None], jnp.exp(scores - log_total), 0.0)
        probs = weights.astype(jnp.bfloat16)
        attended = jnp.einsum("hqk,khd->qhd", weights, value_heads.astype(jnp.float32))
        delta = jnp.sum(grad_heads.astype(jnp.float32) * attended, axis=-1).T
        dprobs = jnp.einsum(
            "qhd,khd->hqk", grad_heads, value_heads, preferred_element_type=jnp.float32
        )
        dscores = (probs.astype(jnp.float32) * (dprobs - delta[:, :, None])).astype(jnp.bfloat16)
        groups = lax.axis_size("col")
        dscores_blocks = jnp.transpose(
            dscores.reshape(local_heads, count, groups, all_tokens // groups), (2, 0, 1, 3)
        )
        dbias_cells = lax.all_to_all(dscores_blocks, "col", split_axis=0, concat_axis=0, tiled=True)
        dbias_parts.append(dbias_cells.reshape(groups * local_heads, count, all_tokens // groups))
        query_grads.append(
            jnp.einsum("hqk,khd->qhd", dscores, key_heads, preferred_element_type=jnp.float32)
            * scale_factor
        )
        key_add = (
            jnp.einsum("hqk,qhd->khd", dscores, query_heads, preferred_element_type=jnp.float32)
            * scale_factor
        )
        value_add = jnp.einsum(
            "hqk,qhd->khd", probs, grad_heads, preferred_element_type=jnp.float32
        )
        kv_parts.append(
            jnp.stack(
                [key_add.reshape(all_tokens, local_width), value_add.reshape(all_tokens, local_width)]
            )
        )
    kv_part = kv_parts[0]
    for extra in kv_parts[1:]:
        kv_part = kv_part + extra
    kv_grads = lax.psum_scatter(kv_part, "blk", scatter_dimension=1, tiled=True)
    grad_queries = jnp.concatenate(query_grads, axis=0).reshape(tok_rows, local_width)
    grad_queries = grad_queries.astype(jnp.bfloat16)
    grad_keys = kv_grads[0].astype(jnp.bfloat16)
    grad_values = kv_grads[1].astype(jnp.bfloat16)

    grad_pair = None
    weight_part = 0.0
    gain_part = 0.0
    for first, dbias_cells in zip(firsts, dbias_parts):
        grad_pair, weight_add, gain_add = pair_grads(
            pair_rep, dbias_cells, norm_gain, bias_weight, first, grad_pair
        )
        weight_part = weight_part + weight_add
        gain_part = gain_part + gain_add
    pair_width = gain_part.shape[1]
    packed = jnp.concatenate([gain_part[0], weight_part.T.reshape(-1)])
    everyone = ("blk", "col")
    devices = lax.axis_size(everyone)
    pieces = lax.all_to_all(packed.reshape(devices, -1), everyone, 0, 0, tiled=True)
    piece = jnp.sum(pieces, axis=0, keepdims=True)
    spread = jnp.broadcast_to(piece, (devices, piece.shape[1]))
    packed = lax.all_to_all(spread, everyone, 0, 0, tiled=True).reshape(-1)
    grad_gain = packed[:pair_width]
    grad_weight = packed[pair_width:].reshape(weight_part.shape[::-1])
    return (grad_queries, grad_keys, grad_values, grad_pair, grad_gain, grad_weight)


def solution(mesh):
    placed = (
        P("blk", "col"),
        P("blk", "col"),
        P("blk", "col"),
        P("blk", "col"),
        P("blk", "col", None),
        P(),
        P(),
        P(),
        P(),
    )
    return jax.shard_map(
        local,
        mesh=mesh,
        in_specs=placed,
        out_specs=(
            P("blk", "col"),
            P("blk", "col"),
            P("blk", "col"),
            P("blk", "col", None),
            P(),
            P(),
        ),
        check_vma=False,
    )
```

```python
import math

import jax
import jax.numpy as jnp
from jax import lax
from jax.experimental import pallas as pl
from jax.experimental.pallas import tpu as pltpu
from jax.sharding import PartitionSpec as P

HEAD_DIM = 24
MASK_BLOCK = 128
ROWS_PER_STEP = 16
CHUNKS = 1


def _norm_rows(x, gain):
    centre = jnp.mean(x, axis=-1, keepdims=True)
    shifted = x - centre
    inverse = lax.rsqrt(jnp.mean(shifted * shifted, axis=-1, keepdims=True) + 1e-05)
    unit = shifted * inverse
    return unit, inverse, (unit * gain).astype(jnp.bfloat16)


def _bias_kernel(pair_ref, gain_ref, wt_ref, bias_ref):
    gain = gain_ref[...]
    wt = wt_ref[...]
    for r in range(pair_ref.shape[0]):
        _, _, normed = _norm_rows(pair_ref[r].astype(jnp.float32), gain)
        bias = lax.dot_general(
            wt, normed, (((1,), (1,)), ((), ())), preferred_element_type=jnp.float32
        )
        bias_ref[:, r, :] = bias.astype(jnp.bfloat16)


def pair_bias(pair_rep, norm_gain, bias_weight, first, count):
    _, cols, width = pair_rep.shape
    heads = bias_weight.shape[1]
    step = ROWS_PER_STEP
    base = first // step
    return pl.pallas_call(
        _bias_kernel,
        out_shape=jax.ShapeDtypeStruct((heads, count, cols), jnp.bfloat16),
        grid=(count // step,),
        in_specs=[
            pl.BlockSpec((step, cols, width), lambda i: (i + base, 0, 0)),
            pl.BlockSpec((1, width), lambda i: (0, 0)),
            pl.BlockSpec((heads, width), lambda i: (0, 0)),
        ],
        out_specs=pl.BlockSpec((heads, step, cols), lambda i: (0, i, 0)),
        compiler_params=pltpu.CompilerParams(dimension_semantics=("arbitrary",)),
    )(pair_rep, norm_gain.reshape(1, width).astype(jnp.float32), bias_weight.T)


def _grad_kernel(pair_ref, ds_ref, gain_ref, wt_ref, *refs):
    gp_ref, gw_ref, gg_ref = refs[-3:]

    @pl.when(pl.program_id(0) == 0)
    def _():
        gw_ref[...] = jnp.zeros_like(gw_ref)
        gg_ref[...] = jnp.zeros_like(gg_ref)

    gain = gain_ref[...]
    wt = wt_ref[...]
    gw = jnp.zeros(gw_ref.shape, jnp.float32)
    gg = jnp.zeros(gg_ref.shape, jnp.float32)
    for r in range(pair_ref.shape[0]):
        unit, inverse, normed = _norm_rows(pair_ref[r].astype(jnp.float32), gain)
        ds = ds_ref[:, r, :]
        ds_t = ds.astype(jnp.float32).T.astype(jnp.bfloat16)
        dnormed = jnp.dot(ds_t, wt, preferred_element_type=jnp.float32)
        gw = gw + jnp.dot(ds, normed, preferred_element_type=jnp.float32)
        gg = gg + jnp.sum(dnormed * unit, axis=0, keepdims=True)
        scaled = dnormed * gain
        grad = inverse * (
            scaled
            - jnp.mean(scaled, axis=-1, keepdims=True)
            - unit * jnp.mean(scaled * unit, axis=-1, keepdims=True)
        )
        gp_ref[r] = grad.astype(jnp.bfloat16)
    gw_ref[...] += gw
    gg_ref[...] += gg


def pair_grads(pair_rep, dbias, norm_gain, bias_weight, first, into):
    rows, cols, width = pair_rep.shape
    count = dbias.shape[1]
    heads = bias_weight.shape[1]
    step = ROWS_PER_STEP
    base = first // step
    operands = [pair_rep, dbias, norm_gain.reshape(1, width).astype(jnp.float32), bias_weight.T]
    in_specs = [
        pl.BlockSpec((step, cols, width), lambda i: (i + base, 0, 0)),
        pl.BlockSpec((heads, step, cols), lambda i: (0, i, 0)),
        pl.BlockSpec((1, width), lambda i: (0, 0)),
        pl.BlockSpec((heads, width), lambda i: (0, 0)),
    ]
    aliases = {}
    if into is not None:
        aliases = {len(operands): 0}
        operands.append(into)
        in_specs.append(pl.BlockSpec(memory_space=pl.ANY))
    return pl.pallas_call(
        _grad_kernel,
        out_shape=(
            jax.ShapeDtypeStruct((rows, cols, width), jnp.bfloat16),
            jax.ShapeDtypeStruct((heads, width), jnp.float32),
            jax.ShapeDtypeStruct((1, width), jnp.float32),
        ),
        grid=(count // step,),
        in_specs=in_specs,
        out_specs=(
            pl.BlockSpec((step, cols, width), lambda i: (i + base, 0, 0)),
            pl.BlockSpec((heads, width), lambda i: (0, 0)),
            pl.BlockSpec((1, width), lambda i: (0, 0)),
        ),
        input_output_aliases=aliases,
        compiler_params=pltpu.CompilerParams(dimension_semantics=("arbitrary",)),
    )(*operands)


def block_onehot(first_token, count, nblocks):
    block_ids = (first_token + jnp.arange(count, dtype=jnp.int32)) // MASK_BLOCK
    return (block_ids[:, None] == jnp.arange(nblocks, dtype=jnp.int32)[None, :]).astype(
        jnp.bfloat16
    )


def local(
    queries, key_proj, value_proj, out_grad, pair_rep, norm_gain, bias_weight, chain_ids, block_mask
):
    tok_rows = queries.shape[0]
    local_width = queries.shape[1]
    local_heads = local_width // HEAD_DIM
    scale_factor = 1.0 / math.sqrt(HEAD_DIM)
    blk_index = lax.axis_index("blk")
    blk_count = lax.axis_size("blk")
    all_tokens = blk_count * tok_rows
    row_start = blk_index * tok_rows
    nblocks = block_mask.shape[0]
    count = tok_rows // CHUNKS
    firsts = [c * count for c in range(CHUNKS)]

    kv_local = jnp.stack([key_proj, value_proj])
    kv_rep = jnp.broadcast_to(kv_local[None], (blk_count,) + kv_local.shape)
    kv_all = lax.all_to_all(kv_rep, "blk", split_axis=0, concat_axis=0, tiled=True)
    kv_all = jnp.transpose(kv_all, (1, 0, 2, 3)).reshape(2, all_tokens, local_width)
    key_heads = kv_all[0].reshape(all_tokens, local_heads, HEAD_DIM)
    value_heads = kv_all[1].reshape(all_tokens, local_heads, HEAD_DIM)

    bias_parts = []
    for first in firsts:
        bias_local = pair_bias(pair_rep, norm_gain, bias_weight, first, count)
        heads, _, cols = bias_local.shape
        groups = lax.axis_size("col")
        bias_mine = lax.all_to_all(
            bias_local.reshape(groups, heads // groups, count, cols),
            "col", split_axis=0, concat_axis=0, tiled=True,
        )
        bias_mine = jnp.transpose(bias_mine, (1, 2, 0, 3)).reshape(local_heads, count, all_tokens)
        bias_parts.append(bias_mine)

    column_table = block_onehot(0, all_tokens, nblocks)
    query_grads, kv_parts, dbias_parts = [], [], []
    for first, bias_mine in zip(firsts, bias_parts):
        rows_table = jnp.dot(
            block_onehot(row_start + first, count, nblocks),
            block_mask.astype(jnp.bfloat16),
            preferred_element_type=jnp.float32,
        ).astype(jnp.bfloat16)
        chain_rows = lax.dynamic_slice_in_dim(chain_ids, row_start + first, count)
        hits = lax.dot_general(
            rows_table, column_table, (((1,), (1,)), ((), ())), preferred_element_type=jnp.float32
        )
        allowed = (hits > 0.5) | (chain_rows[:, None] == chain_ids[None, :])
        query_heads = queries[first : first + count].reshape(count, local_heads, HEAD_DIM)
        grad_heads = out_grad[first : first + count].reshape(count, local_heads, HEAD_DIM)

        scores = (
            jnp.einsum("qhd,khd->hqk", query_heads, key_heads, preferred_element_type=jnp.float32)
            * scale_factor
            + bias_mine.astype(jnp.float32)
        )
        masked = jnp.where(allowed[None], scores, -jnp.inf)
        row_top = jnp.max(masked, axis=-1, keepdims=True)
        expo = jnp.where(allowed[None], jnp.exp(scores - row_top), 0.0)
        totals = jnp.sum(expo, axis=-1, keepdims=True)
        log_total = row_top + jnp.log(totals)
        weights = jnp.where(allowed[None], jnp.exp(scores - log_total), 0.0)
        probs = weights.astype(jnp.bfloat16)
        attended = jnp.einsum("hqk,khd->qhd", weights, value_heads.astype(jnp.float32))
        delta = jnp.sum(grad_heads.astype(jnp.float32) * attended, axis=-1).T
        dprobs = jnp.einsum(
            "qhd,khd->hqk", grad_heads, value_heads, preferred_element_type=jnp.float32
        )
        dscores = (probs.astype(jnp.float32) * (dprobs - delta[:, :, None])).astype(jnp.bfloat16)
        groups = lax.axis_size("col")
        dscores_blocks = jnp.transpose(
            dscores.reshape(local_heads, count, groups, all_tokens // groups), (2, 0, 1, 3)
        )
        dbias_cells = lax.all_to_all(dscores_blocks, "col", split_axis=0, concat_axis=0, tiled=True)
        dbias_parts.append(dbias_cells.reshape(groups * local_heads, count, all_tokens // groups))
        query_grads.append(
            jnp.einsum("hqk,khd->qhd", dscores, key_heads, preferred_element_type=jnp.float32)
            * scale_factor
        )
        key_add = (
            jnp.einsum("hqk,qhd->khd", dscores, query_heads, preferred_element_type=jnp.float32)
            * scale_factor
        )
        value_add = jnp.einsum(
            "hqk,qhd->khd", probs, grad_heads, preferred_element_type=jnp.float32
        )
        kv_parts.append(
            jnp.stack(
                [key_add.reshape(all_tokens, local_width), value_add.reshape(all_tokens, local_width)]
            )
        )
    kv_part = kv_parts[0]
    for extra in kv_parts[1:]:
        kv_part = kv_part + extra
    kv_grads = lax.psum_scatter(kv_part, "blk", scatter_dimension=1, tiled=True)
    grad_queries = jnp.concatenate(query_grads, axis=0).reshape(tok_rows, local_width)
    grad_queries = grad_queries.astype(jnp.bfloat16)
    grad_keys = kv_grads[0].astype(jnp.bfloat16)
    grad_values = kv_grads[1].astype(jnp.bfloat16)

    grad_pair = None
    weight_part = 0.0
    gain_part = 0.0
    for first, dbias_cells in zip(firsts, dbias_parts):
        grad_pair, weight_add, gain_add = pair_grads(
            pair_rep, dbias_cells, norm_gain, bias_weight, first, grad_pair
        )
        weight_part = weight_part + weight_add
        gain_part = gain_part + gain_add
    pair_width = gain_part.shape[1]
    packed = jnp.concatenate([gain_part[0], weight_part.T.reshape(-1)])
    everyone = ("blk", "col")
    devices = lax.axis_size(everyone)
    spread = jnp.broadcast_to(packed[None], (devices, packed.shape[0]))
    packed = jnp.sum(lax.all_to_all(spread, everyone, 0, 0, tiled=True), axis=0)
    grad_gain = packed[:pair_width]
    grad_weight = packed[pair_width:].reshape(weight_part.shape[::-1])
    return (grad_queries, grad_keys, grad_values, grad_pair, grad_gain, grad_weight)


def solution(mesh):
    placed = (
        P("blk", "col"),
        P("blk", "col"),
        P("blk", "col"),
        P("blk", "col"),
        P("blk", "col", None),
        P(),
        P(),
        P(),
        P(),
    )
    return jax.shard_map(
        local,
        mesh=mesh,
        in_specs=placed,
        out_specs=(
            P("blk", "col"),
            P("blk", "col"),
            P("blk", "col"),
            P("blk", "col", None),
            P(),
            P(),
        ),
        check_vma=False,
    )
```

```python
import math

import jax
import jax.numpy as jnp
from jax import lax
from jax.experimental import pallas as pl
from jax.experimental.pallas import tpu as pltpu
from jax.sharding import PartitionSpec as P

HEAD_DIM = 24
MASK_BLOCK = 128
ROWS_PER_STEP = 16
CHUNKS = 1


def _norm_rows(x, gain):
    centre = jnp.mean(x, axis=-1, keepdims=True)
    shifted = x - centre
    inverse = lax.rsqrt(jnp.mean(shifted * shifted, axis=-1, keepdims=True) + 1e-05)
    unit = shifted * inverse
    return unit, inverse, (unit * gain).astype(jnp.bfloat16)


def _bias_kernel(pair_ref, gain_ref, wt_ref, bias_ref):
    gain = gain_ref[...]
    wt = wt_ref[...]
    for r in range(pair_ref.shape[0]):
        _, _, normed = _norm_rows(pair_ref[r].astype(jnp.float32), gain)
        bias = lax.dot_general(
            wt, normed, (((1,), (1,)), ((), ())), preferred_element_type=jnp.float32
        )
        bias_ref[:, r, :] = bias.astype(jnp.bfloat16)


def pair_bias(pair_rep, norm_gain, bias_weight, first, count):
    _, cols, width = pair_rep.shape
    heads = bias_weight.shape[1]
    step = ROWS_PER_STEP
    base = first // step
    return pl.pallas_call(
        _bias_kernel,
        out_shape=jax.ShapeDtypeStruct((heads, count, cols), jnp.bfloat16),
        grid=(count // step,),
        in_specs=[
            pl.BlockSpec((step, cols, width), lambda i: (i + base, 0, 0)),
            pl.BlockSpec((1, width), lambda i: (0, 0)),
            pl.BlockSpec((heads, width), lambda i: (0, 0)),
        ],
        out_specs=pl.BlockSpec((heads, step, cols), lambda i: (0, i, 0)),
        compiler_params=pltpu.CompilerParams(dimension_semantics=("arbitrary",)),
    )(pair_rep, norm_gain.reshape(1, width).astype(jnp.float32), bias_weight.T)


def _grad_kernel(pair_ref, ds_ref, gain_ref, wt_ref, *refs):
    gp_ref, gw_ref, gg_ref = refs[-3:]

    @pl.when(pl.program_id(0) == 0)
    def _():
        gw_ref[...] = jnp.zeros_like(gw_ref)
        gg_ref[...] = jnp.zeros_like(gg_ref)

    gain = gain_ref[...]
    wt = wt_ref[...]
    gw = jnp.zeros(gw_ref.shape, jnp.float32)
    gg = jnp.zeros(gg_ref.shape, jnp.float32)
    for r in range(pair_ref.shape[0]):
        unit, inverse, normed = _norm_rows(pair_ref[r].astype(jnp.float32), gain)
        ds = ds_ref[:, r, :]
        ds_t = ds.astype(jnp.float32).T.astype(jnp.bfloat16)
        dnormed = jnp.dot(ds_t, wt, preferred_element_type=jnp.float32)
        gw = gw + jnp.dot(ds, normed, preferred_element_type=jnp.float32)
        gg = gg + jnp.sum(dnormed * unit, axis=0, keepdims=True)
        scaled = dnormed * gain
        grad = inverse * (
            scaled
            - jnp.mean(scaled, axis=-1, keepdims=True)
            - unit * jnp.mean(scaled * unit, axis=-1, keepdims=True)
        )
        gp_ref[r] = grad.astype(jnp.bfloat16)
    gw_ref[...] += gw
    gg_ref[...] += gg


def pair_grads(pair_rep, dbias, norm_gain, bias_weight, first, into):
    rows, cols, width = pair_rep.shape
    count = dbias.shape[1]
    heads = bias_weight.shape[1]
    step = ROWS_PER_STEP
    base = first // step
    operands = [pair_rep, dbias, norm_gain.reshape(1, width).astype(jnp.float32), bias_weight.T]
    in_specs = [
        pl.BlockSpec((step, cols, width), lambda i: (i + base, 0, 0)),
        pl.BlockSpec((heads, step, cols), lambda i: (0, i, 0)),
        pl.BlockSpec((1, width), lambda i: (0, 0)),
        pl.BlockSpec((heads, width), lambda i: (0, 0)),
    ]
    aliases = {}
    if into is not None:
        aliases = {len(operands): 0}
        operands.append(into)
        in_specs.append(pl.BlockSpec(memory_space=pl.ANY))
    return pl.pallas_call(
        _grad_kernel,
        out_shape=(
            jax.ShapeDtypeStruct((rows, cols, width), jnp.bfloat16),
            jax.ShapeDtypeStruct((heads, width), jnp.float32),
            jax.ShapeDtypeStruct((1, width), jnp.float32),
        ),
        grid=(count // step,),
        in_specs=in_specs,
        out_specs=(
            pl.BlockSpec((step, cols, width), lambda i: (i + base, 0, 0)),
            pl.BlockSpec((heads, width), lambda i: (0, 0)),
            pl.BlockSpec((1, width), lambda i: (0, 0)),
        ),
        input_output_aliases=aliases,
        compiler_params=pltpu.CompilerParams(dimension_semantics=("arbitrary",)),
    )(*operands)


def block_onehot(first_token, count, nblocks):
    block_ids = (first_token + jnp.arange(count, dtype=jnp.int32)) // MASK_BLOCK
    return (block_ids[:, None] == jnp.arange(nblocks, dtype=jnp.int32)[None, :]).astype(
        jnp.bfloat16
    )


def local(
    queries, key_proj, value_proj, out_grad, pair_rep, norm_gain, bias_weight, chain_ids, block_mask
):
    tok_rows = queries.shape[0]
    local_width = queries.shape[1]
    local_heads = local_width // HEAD_DIM
    scale_factor = 1.0 / math.sqrt(HEAD_DIM)
    blk_index = lax.axis_index("blk")
    blk_count = lax.axis_size("blk")
    all_tokens = blk_count * tok_rows
    row_start = blk_index * tok_rows
    nblocks = block_mask.shape[0]
    count = tok_rows // CHUNKS
    firsts = [c * count for c in range(CHUNKS)]

    kv_local = jnp.stack([key_proj, value_proj])
    kv_rep = jnp.broadcast_to(kv_local[None], (blk_count,) + kv_local.shape)
    kv_all = lax.all_to_all(kv_rep, "blk", split_axis=0, concat_axis=0, tiled=True)
    kv_all = jnp.transpose(kv_all, (1, 0, 2, 3)).reshape(2, all_tokens, local_width)
    key_heads = kv_all[0].reshape(all_tokens, local_heads, HEAD_DIM)
    value_heads = kv_all[1].reshape(all_tokens, local_heads, HEAD_DIM)

    bias_parts = []
    for first in firsts:
        bias_local = pair_bias(pair_rep, norm_gain, bias_weight, first, count)
        heads, _, cols = bias_local.shape
        groups = lax.axis_size("col")
        bias_mine = lax.all_to_all(
            bias_local.reshape(groups, heads // groups, count, cols),
            "col", split_axis=0, concat_axis=0, tiled=True,
        )
        bias_mine = jnp.transpose(bias_mine, (1, 2, 0, 3)).reshape(local_heads, count, all_tokens)
        bias_parts.append(bias_mine)

    column_table = block_onehot(0, all_tokens, nblocks)
    query_grads, kv_parts, dbias_parts = [], [], []
    for first, bias_mine in zip(firsts, bias_parts):
        rows_table = jnp.dot(
            block_onehot(row_start + first, count, nblocks),
            block_mask.astype(jnp.bfloat16),
            preferred_element_type=jnp.float32,
        ).astype(jnp.bfloat16)
        chain_rows = lax.dynamic_slice_in_dim(chain_ids, row_start + first, count)
        hits = lax.dot_general(
            rows_table, column_table, (((1,), (1,)), ((), ())), preferred_element_type=jnp.float32
        )
        allowed = (hits > 0.5) | (chain_rows[:, None] == chain_ids[None, :])
        query_heads = queries[first : first + count].reshape(count, local_heads, HEAD_DIM)
        grad_heads = out_grad[first : first + count].reshape(count, local_heads, HEAD_DIM)

        scores = (
            jnp.einsum("qhd,khd->hqk", query_heads, key_heads, preferred_element_type=jnp.float32)
            * scale_factor
            + bias_mine.astype(jnp.float32)
        )
        masked = jnp.where(allowed[None], scores, -jnp.inf)
        row_top = jnp.max(masked, axis=-1, keepdims=True)
        expo = jnp.where(allowed[None], jnp.exp(scores - row_top), 0.0)
        totals = jnp.sum(expo, axis=-1, keepdims=True)
        log_total = row_top + jnp.log(totals)
        weights = jnp.where(allowed[None], jnp.exp(scores - log_total), 0.0)
        probs = weights.astype(jnp.bfloat16)
        attended = jnp.einsum("hqk,khd->qhd", weights, value_heads.astype(jnp.float32))
        delta = jnp.sum(grad_heads.astype(jnp.float32) * attended, axis=-1).T
        dprobs = jnp.einsum(
            "qhd,khd->hqk", grad_heads, value_heads, preferred_element_type=jnp.float32
        )
        dscores = (probs.astype(jnp.float32) * (dprobs - delta[:, :, None])).astype(jnp.bfloat16)
        groups = lax.axis_size("col")
        dscores_blocks = jnp.transpose(
            dscores.reshape(local_heads, count, groups, all_tokens // groups), (2, 0, 1, 3)
        )
        dbias_cells = lax.all_to_all(dscores_blocks, "col", split_axis=0, concat_axis=0, tiled=True)
        dbias_parts.append(dbias_cells.reshape(groups * local_heads, count, all_tokens // groups))
        query_grads.append(
            jnp.einsum("hqk,khd->qhd", dscores, key_heads, preferred_element_type=jnp.float32)
            * scale_factor
        )
        key_add = (
            jnp.einsum("hqk,qhd->khd", dscores, query_heads, preferred_element_type=jnp.float32)
            * scale_factor
        )
        value_add = jnp.einsum(
            "hqk,qhd->khd", probs, grad_heads, preferred_element_type=jnp.float32
        )
        kv_parts.append(
            jnp.stack(
                [key_add.reshape(all_tokens, local_width), value_add.reshape(all_tokens, local_width)]
            )
        )
    kv_part = kv_parts[0]
    for extra in kv_parts[1:]:
        kv_part = kv_part + extra
    kv_blocks = kv_part.reshape(2, blk_count, tok_rows, local_width)
    kv_grads = jnp.sum(lax.all_to_all(kv_blocks, "blk", 1, 1, tiled=True), axis=1)
    grad_queries = jnp.concatenate(query_grads, axis=0).reshape(tok_rows, local_width)
    grad_queries = grad_queries.astype(jnp.bfloat16)
    grad_keys = kv_grads[0].astype(jnp.bfloat16)
    grad_values = kv_grads[1].astype(jnp.bfloat16)

    grad_pair = None
    weight_part = 0.0
    gain_part = 0.0
    for first, dbias_cells in zip(firsts, dbias_parts):
        grad_pair, weight_add, gain_add = pair_grads(
            pair_rep, dbias_cells, norm_gain, bias_weight, first, grad_pair
        )
        weight_part = weight_part + weight_add
        gain_part = gain_part + gain_add
    pair_width = gain_part.shape[1]
    packed = jnp.concatenate([gain_part[0], weight_part.T.reshape(-1)])
    everyone = ("blk", "col")
    devices = lax.axis_size(everyone)
    spread = jnp.broadcast_to(packed[None], (devices, packed.shape[0]))
    packed = jnp.sum(lax.all_to_all(spread, everyone, 0, 0, tiled=True), axis=0)
    grad_gain = packed[:pair_width]
    grad_weight = packed[pair_width:].reshape(weight_part.shape[::-1])
    return (grad_queries, grad_keys, grad_values, grad_pair, grad_gain, grad_weight)


def solution(mesh):
    placed = (
        P("blk", "col"),
        P("blk", "col"),
        P("blk", "col"),
        P("blk", "col"),
        P("blk", "col", None),
        P(),
        P(),
        P(),
        P(),
    )
    return jax.shard_map(
        local,
        mesh=mesh,
        in_specs=placed,
        out_specs=(
            P("blk", "col"),
            P("blk", "col"),
            P("blk", "col"),
            P("blk", "col", None),
            P(),
            P(),
        ),
        check_vma=False,
    )
```
